32 devices in a mesh: groups: 2 (over x), cell: 16 (over z, y, core).
Axes of the slice: x: 2, y: 2, z: 4, core: 2. Of those that a mesh axis runs over, the one named last changes fastest.
Arguments:
- cells: bfloat16 [256, 64, 768], P(('groups', 'cell')), parts along dimension 0, may hold values from -6 to 6
- cotangent: bfloat16 [256, 64, 768], P('groups', 'cell'), parts along dimension 0, may hold values from -6 to 6
- row_weight: bfloat16 [768, 3072], replicated, may hold values from -0.21875 to 0.21875
- col_weight: bfloat16 [768, 3072], replicated, may hold values from -0.21875 to 0.21875
Outputs:
- grad_cells: bfloat16 [256, 64, 768], P(('groups', 'cell')), parts along dimension 0
- row_grad: float32 [1536, 3072], P(('groups', 'cell')), parts along dimension 0
- col_grad: float32 [1536, 3072], P(('groups', 'cell')), parts along dimension 0
The draws below stay inside these ranges and needn't reach their ends.
There are 2 independent parts, one for each index of `groups`. The reference program is written for one: setup_inputs(seed, part) draws one part's arguments, and reference() takes and returns one part's arrays. A program takes and returns all parts, laid end to end along the dimension named above; an argument that names none is the same for every part. Nothing has to cross between parts.
All inputs are finite; a program needn't handle non-finite values.
Results may differ from the reference program's by a relative error of at most 0.012.
Values may be sent and summed in bfloat16 or wider, within the bound.
No kernel may reach another device: no remote copies, remote signals or barrier semaphores. Data moves between devices by JAX's collectives and lax.ppermute only.
A program may use at most 128 MiB of HBM per device.

```python
import jax
import jax.numpy as jnp
from jax import lax

D = 768
HEADS = 12
C = 64
ROWS = 128


def steps_of(key, dims, shards, smallest, top_value):
    gain, own = 1.0, jax.random.fold_in(key, 6)
    for position, parts in shards:
        steps = jnp.exp(jax.random.uniform(jax.random.fold_in(own, position), (parts,), jnp.float32, smallest / len(shards), top_value / len(shards)))
        gain = gain * jnp.repeat(steps, dims[position] // parts).reshape([-1 if axis == position else 1 for axis in range(len(dims))])
    return gain


def bell_draw(own_key, shape, scale, bound, pieces=(), dtype=jnp.bfloat16):
    loudness = steps_of(own_key, shape, pieces, -0.22, 0.18) if pieces else 1.0
    drawn = jax.random.normal(own_key, shape, jnp.float32) * scale * loudness
    return jnp.minimum(jnp.maximum(drawn, -bound), bound).astype(dtype)


def setup_inputs(seed: int = 0, part: int = 0) -> dict:
    key_of = jax.random.split(jax.random.key(seed), 5)
    own_keys = jax.random.split(jax.random.fold_in(key_of[4], part), 5)
    return {
        "cells": bell_draw(own_keys[0], (ROWS, C, D), 1.0, 6.0, ((0, 16),)),
        "cotangent": bell_draw(own_keys[1], (ROWS, C, D), 1.0, 6.0, ((1, 16),)),
        "row_weight": bell_draw(key_of[2], (D, 4 * D), D ** -0.5, 0.21875),
        "col_weight": bell_draw(key_of[3], (D, 4 * D), D ** -0.5, 0.21875),
    }


EPS = 1e-06

def normalize(values):
    return values * lax.rsqrt(lax.optimization_barrier(jnp.mean(values * values, axis=-1, keepdims=True)) + EPS)

def attend(packed, attn_dim):
    model_width = packed.shape[-1] // 3
    head_size = model_width // HEADS
    split_shape = packed.shape[:-1] + (HEADS, head_size)
    queries = packed[..., :model_width].reshape(split_shape)
    keys_part = packed[..., model_width:2 * model_width].reshape(split_shape)
    values_part = packed[..., 2 * model_width:].reshape(split_shape)
    if attn_dim == 1:
        forms = ('blhe,bmhe->bhlm', 'bhlm,bmhe->blhe')
    else:
        forms = ('lbhe,mbhe->bhlm', 'bhlm,mbhe->lbhe')
    scores = jnp.einsum(forms[0], queries, keys_part, preferred_element_type=jnp.float32) * head_size ** (-0.5)
    weights = jax.nn.softmax(scores, axis=-1).astype(jnp.bfloat16)
    mixture = jnp.einsum(forms[1], weights, values_part, preferred_element_type=jnp.float32)
    return mixture.reshape(packed.shape[:-1] + (model_width,)).astype(jnp.bfloat16)

def forward(cells_in, weight, attn_dim):
    model_width = weight.shape[0]
    inputs_f = cells_in.astype(jnp.float32)
    normed = normalize(inputs_f).astype(jnp.bfloat16)
    projected = jnp.dot(normed, weight[:, :3 * model_width], preferred_element_type=jnp.float32).astype(jnp.bfloat16)
    attended = attend(projected, attn_dim)
    result = (inputs_f + jnp.dot(attended, weight[:, 3 * model_width:], preferred_element_type=jnp.float32)).astype(jnp.bfloat16)
    return (inputs_f, normed, projected, attended, result)

def backward(saved, weight, upstream, attn_dim):
    inputs_f, normed, projected, attended, result = saved
    model_width = weight.shape[0]
    grad_attended = jnp.dot(upstream, weight[:, 3 * model_width:].T, preferred_element_type=jnp.float32).astype(jnp.bfloat16)
    unused, pull = jax.vjp(lambda packed: attend(packed, attn_dim), projected)
    grad_projected = pull(grad_attended)[0].astype(jnp.bfloat16)
    grad_normed = jnp.dot(grad_projected, weight[:, :3 * model_width].T, preferred_element_type=jnp.float32)
    unused_norm, pull_norm = jax.vjp(normalize, inputs_f)
    grad_input = (upstream.astype(jnp.float32) + pull_norm(grad_normed)[0]).astype(jnp.bfloat16)
    return (grad_input, grad_projected)

def weight_term(normed, grad_projected, attended, upstream):
    last = normed.ndim - 1
    leading = tuple(range(last))
    first = lax.dot_general(normed, grad_projected, ((leading, leading), ((), ())), preferred_element_type=jnp.float32)
    second = lax.dot_general(attended, upstream, ((leading, leading), ((), ())), preferred_element_type=jnp.float32)
    return jnp.concatenate([first, second], axis=1)

def reference(cells, cotangent, row_weight, col_weight):
    row_saved = forward(cells, row_weight, 1)
    col_saved = forward(row_saved[4], col_weight, 0)
    grad_mid, grad_col_proj = backward(col_saved, col_weight, cotangent, 0)
    grad_cells, grad_row_proj = backward(row_saved, row_weight, grad_mid, 1)
    col_grad = weight_term(col_saved[1], grad_col_proj, col_saved[3], cotangent)
    row_grad = weight_term(row_saved[1], grad_row_proj, row_saved[3], grad_mid)
    return (grad_cells, row_grad, col_grad)
```

```python
import jax
import jax.numpy as jnp
from jax import lax
from jax.sharding import PartitionSpec as P

HEADS = 12


EPS = 1e-06


def normalize(values):
    return values * lax.rsqrt(jnp.mean(values * values, axis=-1, keepdims=True) + EPS)


def attend(packed, attn_dim):
    model_width = packed.shape[-1] // 3
    head_size = model_width // HEADS
    split_shape = packed.shape[:-1] + (HEADS, head_size)
    queries = packed[..., :model_width].reshape(split_shape)
    keys_part = packed[..., model_width : 2 * model_width].reshape(split_shape)
    values_part = packed[..., 2 * model_width :].reshape(split_shape)
    if attn_dim == 1:
        forms = ("blhe,bmhe->bhlm", "bhlm,bmhe->blhe")
    else:
        forms = ("lbhe,mbhe->bhlm", "bhlm,mbhe->lbhe")
    scores = jnp.einsum(
        forms[0], queries, keys_part, preferred_element_type=jnp.float32
    ) * head_size ** (-0.5)
    weights = jax.nn.softmax(scores, axis=-1).astype(jnp.bfloat16)
    mixture = jnp.einsum(forms[1], weights, values_part, preferred_element_type=jnp.float32)
    return mixture.reshape(packed.shape[:-1] + (model_width,)).astype(jnp.bfloat16)


def forward(cells_in, weight, attn_dim):
    model_width = weight.shape[0]
    inputs_f = cells_in.astype(jnp.float32)
    normed = normalize(inputs_f).astype(jnp.bfloat16)
    projected = jnp.dot(
        normed, weight[:, : 3 * model_width], preferred_element_type=jnp.float32
    ).astype(jnp.bfloat16)
    attended = attend(projected, attn_dim)
    result = (
        inputs_f
        + jnp.dot(attended, weight[:, 3 * model_width :], preferred_element_type=jnp.float32)
    ).astype(jnp.bfloat16)
    return (inputs_f, normed, projected, attended, result)


def backward(saved, weight, upstream, attn_dim):
    inputs_f, normed, projected, attended, result = saved
    model_width = weight.shape[0]
    grad_attended = jnp.dot(
        upstream, weight[:, 3 * model_width :].T, preferred_element_type=jnp.float32
    ).astype(jnp.bfloat16)
    unused, pull = jax.vjp(lambda packed: attend(packed, attn_dim), projected)
    grad_projected = pull(grad_attended)[0]
    grad_normed = jnp.dot(
        grad_projected, weight[:, : 3 * model_width].T, preferred_element_type=jnp.float32
    )
    unused_norm, pull_norm = jax.vjp(normalize, inputs_f)
    grad_input = (upstream.astype(jnp.float32) + pull_norm(grad_normed)[0]).astype(jnp.bfloat16)
    return (grad_input, grad_projected)


def weight_term(normed, grad_projected, attended, upstream):
    last = normed.ndim - 1
    leading = tuple(range(last))
    first = lax.dot_general(
        normed, grad_projected, ((leading, leading), ((), ())), preferred_element_type=jnp.float32
    )
    second = lax.dot_general(
        attended, upstream, ((leading, leading), ((), ())), preferred_element_type=jnp.float32
    )
    return jnp.concatenate([first, second], axis=1)


def body(cells, cotangent, row_weight, col_weight):
    row_saved = forward(cells, row_weight, 1)
    mid_columns = lax.all_to_all(row_saved[4], "cell", split_axis=1, concat_axis=0, tiled=True)
    col_saved = forward(mid_columns, col_weight, 0)
    grad_mid_columns, grad_col_proj = backward(col_saved, col_weight, cotangent, 0)
    col_term = weight_term(col_saved[1], grad_col_proj, col_saved[3], cotangent)
    col_grad = lax.psum_scatter(col_term, "cell", scatter_dimension=0, tiled=True)
    grad_mid = lax.all_to_all(grad_mid_columns, "cell", split_axis=0, concat_axis=1, tiled=True)
    grad_cells, grad_row_proj = backward(row_saved, row_weight, grad_mid, 1)
    row_term = weight_term(row_saved[1], grad_row_proj, row_saved[3], grad_mid)
    row_grad = lax.psum_scatter(row_term, "cell", scatter_dimension=0, tiled=True)
    return (grad_cells, row_grad, col_grad)


def solution(mesh):
    placed = (P(("groups", "cell"), None, None), P("groups", "cell", None), P(), P())
    return jax.shard_map(
        body,
        mesh=mesh,
        in_specs=placed,
        out_specs=(
            P(("groups", "cell"), None, None),
            P(("groups", "cell"), None),
            P(("groups", "cell"), None),
        ),
        check_vma=False,
    )
```

```python
import jax
import jax.numpy as jnp
from jax import lax
from jax.sharding import PartitionSpec as P

HEADS = 12


EPS = 1e-06


def normalize(values):
    return values * lax.rsqrt(jnp.mean(values * values, axis=-1, keepdims=True) + EPS)


def attend(packed, attn_dim):
    model_width = packed.shape[-1] // 3
    head_size = model_width // HEADS
    split_shape = packed.shape[:-1] + (HEADS, head_size)
    queries = packed[..., :model_width].reshape(split_shape)
    keys_part = packed[..., model_width : 2 * model_width].reshape(split_shape)
    values_part = packed[..., 2 * model_width :].reshape(split_shape)
    if attn_dim == 1:
        forms = ("blhe,bmhe->bhlm", "bhlm,bmhe->blhe")
    else:
        forms = ("lbhe,mbhe->bhlm", "bhlm,mbhe->lbhe")
    scores = jnp.einsum(
        forms[0], queries, keys_part, preferred_element_type=jnp.float32
    ) * head_size ** (-0.5)
    weights = jax.nn.softmax(scores, axis=-1).astype(jnp.bfloat16)
    mixture = jnp.einsum(forms[1], weights, values_part, preferred_element_type=jnp.float32)
    return mixture.reshape(packed.shape[:-1] + (model_width,)).astype(jnp.bfloat16)


def forward(cells_in, weight, attn_dim):
    model_width = weight.shape[0]
    inputs_f = cells_in.astype(jnp.float32)
    normed = normalize(inputs_f).astype(jnp.bfloat16)
    projected = jnp.dot(
        normed, weight[:, : 3 * model_width], preferred_element_type=jnp.float32
    ).astype(jnp.bfloat16)
    attended = attend(projected, attn_dim)
    result = (
        inputs_f
        + jnp.dot(attended, weight[:, 3 * model_width :], preferred_element_type=jnp.float32)
    ).astype(jnp.bfloat16)
    return (inputs_f, normed, projected, attended, result)


def backward(saved, weight, upstream, attn_dim):
    inputs_f, normed, projected, attended, result = saved
    model_width = weight.shape[0]
    grad_attended = jnp.dot(
        upstream, weight[:, 3 * model_width :].T, preferred_element_type=jnp.float32
    ).astype(jnp.bfloat16)
    unused, pull = jax.vjp(lambda packed: attend(packed, attn_dim), projected)
    grad_projected = pull(grad_attended)[0]
    grad_normed = jnp.dot(
        grad_projected, weight[:, : 3 * model_width].T, preferred_element_type=jnp.float32
    )
    unused_norm, pull_norm = jax.vjp(normalize, inputs_f)
    grad_input = (upstream.astype(jnp.float32) + pull_norm(grad_normed)[0]).astype(jnp.bfloat16)
    return (grad_input, grad_projected)


def weight_term(normed, grad_projected, attended, upstream):
    last = normed.ndim - 1
    leading = tuple(range(last))
    first = lax.dot_general(
        normed, grad_projected, ((leading, leading), ((), ())), preferred_element_type=jnp.float32
    )
    second = lax.dot_general(
        attended, upstream, ((leading, leading), ((), ())), preferred_element_type=jnp.float32
    )
    return jnp.concatenate([first, second], axis=1)


def body(cells, cotangent, row_weight, col_weight):
    row_saved = forward(cells, row_weight, 1)
    mid_columns = lax.all_to_all(row_saved[4], "cell", split_axis=1, concat_axis=0, tiled=True)
    col_saved = forward(mid_columns, col_weight, 0)
    grad_mid_columns, grad_col_proj = backward(col_saved, col_weight, cotangent, 0)
    col_term = weight_term(col_saved[1], grad_col_proj, col_saved[3], cotangent)
    col_grad = lax.psum_scatter(
        col_term.astype(jnp.bfloat16), "cell", scatter_dimension=0, tiled=True
    ).astype(jnp.float32)
    grad_mid = lax.all_to_all(grad_mid_columns, "cell", split_axis=0, concat_axis=1, tiled=True)
    grad_cells, grad_row_proj = backward(row_saved, row_weight, grad_mid, 1)
    row_term = weight_term(row_saved[1], grad_row_proj, row_saved[3], grad_mid)
    row_grad = lax.psum_scatter(
        row_term.astype(jnp.bfloat16), "cell", scatter_dimension=0, tiled=True
    ).astype(jnp.float32)
    return (grad_cells, row_grad, col_grad)


def solution(mesh):
    placed = (P(("groups", "cell"), None, None), P("groups", "cell", None), P(), P())
    return jax.shard_map(
        body,
        mesh=mesh,
        in_specs=placed,
        out_specs=(
            P(("groups", "cell"), None, None),
            P(("groups", "cell"), None),
            P(("groups", "cell"), None),
        ),
        check_vma=False,
    )
```

```python
import jax
import jax.numpy as jnp
from jax import lax
from jax.sharding import PartitionSpec as P

HEADS = 12


EPS = 1e-06


def normalize(values):
    return values * lax.rsqrt(jnp.mean(values * values, axis=-1, keepdims=True) + EPS)


def attend_heads(queries, keys_part, values_part):
    head_size = queries.shape[-1]
    scores = jnp.einsum(
        "bhle,bhme->bhlm", queries, keys_part, preferred_element_type=jnp.float32
    ) * head_size ** (-0.5)
    weights = jax.nn.softmax(scores, axis=-1).astype(jnp.bfloat16)
    mixture = jnp.einsum("bhlm,bhme->bhle", weights, values_part, preferred_element_type=jnp.float32)
    return mixture.astype(jnp.bfloat16)


def forms_of(attn_dim):
    return "bld" if attn_dim == 1 else "lbd", "blf" if attn_dim == 1 else "lbf"


def split_weight(weight):
    model_width = weight.shape[0]
    head_size = model_width // HEADS
    projection = weight[:, : 3 * model_width].reshape(model_width, 3, HEADS, head_size)
    output = weight[:, 3 * model_width :].reshape(HEADS, head_size, model_width)
    return projection, output


def forward(cells_in, weight, attn_dim, with_result):
    cell_form, out_form = forms_of(attn_dim)
    projection, output = split_weight(weight)
    inputs_f = cells_in.astype(jnp.float32)
    normed = normalize(inputs_f).astype(jnp.bfloat16)
    projected = jnp.einsum(
        cell_form + ",dthe->tbhle", normed, projection, preferred_element_type=jnp.float32
    ).astype(jnp.bfloat16)
    attended = attend_heads(projected[0], projected[1], projected[2])
    result = None
    if with_result:
        result = (
            inputs_f
            + jnp.einsum("bhle,hef->" + out_form, attended, output, preferred_element_type=jnp.float32)
        ).astype(jnp.bfloat16)
    return (inputs_f, normed, projected, attended, result)


def backward(saved, weight, upstream, attn_dim):
    inputs_f, normed, projected, attended, result = saved
    cell_form, out_form = forms_of(attn_dim)
    projection, output = split_weight(weight)
    grad_attended = jnp.einsum(
        out_form + ",hef->bhle", upstream, output, preferred_element_type=jnp.float32
    ).astype(jnp.bfloat16)
    unused, pull = jax.vjp(attend_heads, projected[0], projected[1], projected[2])
    grad_projected = jnp.stack(pull(grad_attended)).astype(jnp.bfloat16)
    grad_normed = jnp.einsum(
        "tbhle,dthe->" + cell_form, grad_projected, projection, preferred_element_type=jnp.float32
    )
    unused_norm, pull_norm = jax.vjp(normalize, inputs_f)
    grad_input = (upstream.astype(jnp.float32) + pull_norm(grad_normed)[0]).astype(jnp.bfloat16)
    return (grad_input, grad_projected)


def weight_term(normed, grad_projected, attended, upstream, attn_dim):
    cell_form, out_form = forms_of(attn_dim)
    model_width = normed.shape[-1]
    first = jnp.einsum(
        cell_form + ",tbhle->dthe", normed, grad_projected, preferred_element_type=jnp.float32
    ).reshape(model_width, 3 * model_width)
    second = jnp.einsum(
        "bhle," + out_form + "->hef", attended, upstream, preferred_element_type=jnp.float32
    ).reshape(model_width, model_width)
    return jnp.concatenate([first, second], axis=1)


def body(cells, cotangent, row_weight, col_weight):
    row_saved = forward(cells, row_weight, 1, True)
    mid_columns = lax.all_to_all(row_saved[4], "cell", split_axis=1, concat_axis=0, tiled=True)
    col_saved = forward(mid_columns, col_weight, 0, False)
    grad_mid_columns, grad_col_proj = backward(col_saved, col_weight, cotangent, 0)
    col_term = weight_term(col_saved[1], grad_col_proj, col_saved[3], cotangent, 0)
    col_grad = lax.psum_scatter(
        col_term.astype(jnp.bfloat16), "cell", scatter_dimension=0, tiled=True
    ).astype(jnp.float32)
    grad_mid = lax.all_to_all(grad_mid_columns, "cell", split_axis=0, concat_axis=1, tiled=True)
    grad_cells, grad_row_proj = backward(row_saved, row_weight, grad_mid, 1)
    row_term = weight_term(row_saved[1], grad_row_proj, row_saved[3], grad_mid, 1)
    row_grad = lax.psum_scatter(
        row_term.astype(jnp.bfloat16), "cell", scatter_dimension=0, tiled=True
    ).astype(jnp.float32)
    return (grad_cells, row_grad, col_grad)


def solution(mesh):
    placed = (P(("groups", "cell"), None, None), P("groups", "cell", None), P(), P())
    return jax.shard_map(
        body,
        mesh=mesh,
        in_specs=placed,
        out_specs=(
            P(("groups", "cell"), None, None),
            P(("groups", "cell"), None),
            P(("groups", "cell"), None),
        ),
        check_vma=False,
    )
```

```python
import jax
import jax.numpy as jnp
from jax import lax
from jax.sharding import PartitionSpec as P

HEADS = 12


EPS = 1e-06


def normalize(values):
    return values * lax.rsqrt(jnp.mean(values * values, axis=-1, keepdims=True) + EPS)


def attend_heads(queries, keys_part, values_part):
    head_size = queries.shape[-1]
    scores = jnp.einsum(
        "bhle,bhme->bhlm", queries, keys_part, preferred_element_type=jnp.float32
    ) * head_size ** (-0.5)
    weights = jax.nn.softmax(scores, axis=-1).astype(jnp.bfloat16)
    mixture = jnp.einsum("bhlm,bhme->bhle", weights, values_part, preferred_element_type=jnp.float32)
    return mixture.astype(jnp.bfloat16)


def forms_of(attn_dim):
    return "bld" if attn_dim == 1 else "lbd", "blf" if attn_dim == 1 else "lbf"


def split_weight(weight):
    model_width = weight.shape[0]
    head_size = model_width // HEADS
    projection = weight[:, : 3 * model_width].reshape(model_width, 3, HEADS, head_size)
    output = weight[:, 3 * model_width :].reshape(HEADS, head_size, model_width)
    return projection, output


def forward(cells_in, weight, attn_dim, with_result):
    cell_form, out_form = forms_of(attn_dim)
    projection, output = split_weight(weight)
    inputs_f = cells_in.astype(jnp.float32)
    normed = normalize(inputs_f).astype(jnp.bfloat16)
    projected = jnp.einsum(
        cell_form + ",dthe->tbhle", normed, projection, preferred_element_type=jnp.float32
    ).astype(jnp.bfloat16)
    attended = attend_heads(projected[0], projected[1], projected[2])
    result = None
    if with_result:
        result = (
            inputs_f
            + jnp.einsum("bhle,hef->" + out_form, attended, output, preferred_element_type=jnp.float32)
        ).astype(jnp.bfloat16)
    return (inputs_f, normed, projected, attended, result)


def backward(saved, weight, upstream, attn_dim):
    inputs_f, normed, projected, attended, result = saved
    cell_form, out_form = forms_of(attn_dim)
    projection, output = split_weight(weight)
    grad_attended = jnp.einsum(
        out_form + ",hef->bhle", upstream, output, preferred_element_type=jnp.float32
    ).astype(jnp.bfloat16)
    unused, pull = jax.vjp(attend_heads, projected[0], projected[1], projected[2])
    grad_projected = jnp.stack(pull(grad_attended)).astype(jnp.bfloat16)
    grad_normed = jnp.einsum(
        "tbhle,dthe->" + cell_form, grad_projected, projection, preferred_element_type=jnp.float32
    )
    unused_norm, pull_norm = jax.vjp(normalize, inputs_f)
    grad_input = (upstream.astype(jnp.float32) + pull_norm(grad_normed)[0]).astype(jnp.bfloat16)
    return (grad_input, grad_projected)


def weight_term(normed, grad_projected, attended, upstream, attn_dim):
    cell_form, out_form = forms_of(attn_dim)
    model_width = normed.shape[-1]
    first = jnp.einsum(
        cell_form + ",tbhle->dthe", normed, grad_projected, preferred_element_type=jnp.float32
    ).reshape(model_width, 3 * model_width)
    second = jnp.einsum(
        "bhle," + out_form + "->hef", attended, upstream, preferred_element_type=jnp.float32
    ).reshape(model_width, model_width)
    return jnp.concatenate([first, second], axis=1)


def halving_scatter(term, axis_name):
    count = lax.axis_size(axis_name)
    if count & (count - 1):
        return lax.psum_scatter(
            term.astype(jnp.bfloat16), axis_name, scatter_dimension=0, tiled=True
        ).astype(jnp.float32)
    index = lax.axis_index(axis_name)
    block = term.shape[0] // count
    current = term.reshape((count, block) + term.shape[1:])
    step = 0
    while current.shape[0] > 1:
        pairs = current.reshape((current.shape[0] // 2, 2) + current.shape[1:])
        mine = (index >> step) & 1
        keep = lax.dynamic_index_in_dim(pairs, mine, axis=1, keepdims=False)
        send = lax.dynamic_index_in_dim(pairs, 1 - mine, axis=1, keepdims=False)
        partner = [(i, i ^ (1 << step)) for i in range(count)]
        received = lax.ppermute(send.astype(jnp.bfloat16), axis_name, perm=partner)
        current = keep + received.astype(jnp.float32)
        step += 1
    return current.reshape(term.shape[:0] + (block,) + term.shape[1:])


def body(cells, cotangent, row_weight, col_weight):
    row_saved = forward(cells, row_weight, 1, True)
    mid_columns = lax.all_to_all(row_saved[4], "cell", split_axis=1, concat_axis=0, tiled=True)
    col_saved = forward(mid_columns, col_weight, 0, False)
    grad_mid_columns, grad_col_proj = backward(col_saved, col_weight, cotangent, 0)
    col_term = weight_term(col_saved[1], grad_col_proj, col_saved[3], cotangent, 0)
    col_term, grad_mid_columns = lax.optimization_barrier((col_term, grad_mid_columns))
    col_grad = halving_scatter(col_term, "cell")
    grad_mid = lax.all_to_all(grad_mid_columns, "cell", split_axis=0, concat_axis=1, tiled=True)
    grad_cells, grad_row_proj = backward(row_saved, row_weight, grad_mid, 1)
    row_term = weight_term(row_saved[1], grad_row_proj, row_saved[3], grad_mid, 1)
    row_grad = halving_scatter(row_term, "cell")
    return (grad_cells, row_grad, col_grad)


def solution(mesh):
    placed = (P(("groups", "cell"), None, None), P("groups", "cell", None), P(), P())
    return jax.shard_map(
        body,
        mesh=mesh,
        in_specs=placed,
        out_specs=(
            P(("groups", "cell"), None, None),
            P(("groups", "cell"), None),
            P(("groups", "cell"), None),
        ),
        check_vma=False,
    )
```

```python
import jax
import jax.numpy as jnp
from jax import lax
from jax.sharding import PartitionSpec as P

HEADS = 12


EPS = 1e-06


def normalize(values):
    return values * lax.rsqrt(jnp.mean(values * values, axis=-1, keepdims=True) + EPS)


def attend_heads(queries, keys_part, values_part):
    head_size = queries.shape[-1]
    scores = jnp.einsum(
        "bhle,bhme->bhlm", queries, keys_part, preferred_element_type=jnp.float32
    ) * head_size ** (-0.5)
    weights = jax.nn.softmax(scores, axis=-1).astype(jnp.bfloat16)
    mixture = jnp.einsum("bhlm,bhme->bhle", weights, values_part, preferred_element_type=jnp.float32)
    return mixture.astype(jnp.bfloat16)


def forms_of(attn_dim):
    return "bld" if attn_dim == 1 else "lbd", "blf" if attn_dim == 1 else "lbf"


def split_weight(weight):
    model_width = weight.shape[0]
    head_size = model_width // HEADS
    projection = weight[:, : 3 * model_width].reshape(model_width, 3, HEADS, head_size)
    output = weight[:, 3 * model_width :].reshape(HEADS, head_size, model_width)
    return projection, output


def forward(cells_in, weight, attn_dim, with_result):
    cell_form, out_form = forms_of(attn_dim)
    projection, output = split_weight(weight)
    inputs_f = cells_in.astype(jnp.float32)
    normed = normalize(inputs_f).astype(jnp.bfloat16)
    projected = jnp.einsum(
        cell_form + ",dthe->tbhle", normed, projection, preferred_element_type=jnp.float32
    ).astype(jnp.bfloat16)
    attended = attend_heads(projected[0], projected[1], projected[2])
    result = None
    if with_result:
        result = (
            inputs_f
            + jnp.einsum("bhle,hef->" + out_form, attended, output, preferred_element_type=jnp.float32)
        ).astype(jnp.bfloat16)
    return (inputs_f, normed, projected, attended, result)


def backward(saved, weight, upstream, attn_dim):
    inputs_f, normed, projected, attended, result = saved
    cell_form, out_form = forms_of(attn_dim)
    projection, output = split_weight(weight)
    grad_attended = jnp.einsum(
        out_form + ",hef->bhle", upstream, output, preferred_element_type=jnp.float32
    ).astype(jnp.bfloat16)
    unused, pull = jax.vjp(attend_heads, projected[0], projected[1], projected[2])
    grad_projected = jnp.stack(pull(grad_attended)).astype(jnp.bfloat16)
    grad_normed = jnp.einsum(
        "tbhle,dthe->" + cell_form, grad_projected, projection, preferred_element_type=jnp.float32
    )
    unused_norm, pull_norm = jax.vjp(normalize, inputs_f)
    grad_input = (upstream.astype(jnp.float32) + pull_norm(grad_normed)[0]).astype(jnp.bfloat16)
    return (grad_input, grad_projected)


def weight_term(normed, grad_projected, attended, upstream, attn_dim):
    cell_form, out_form = forms_of(attn_dim)
    model_width = normed.shape[-1]
    first = jnp.einsum(
        cell_form + ",tbhle->dthe", normed, grad_projected, preferred_element_type=jnp.float32
    ).reshape(model_width, 3 * model_width)
    second = jnp.einsum(
        "bhle," + out_form + "->hef", attended, upstream, preferred_element_type=jnp.float32
    ).reshape(model_width, model_width)
    return jnp.concatenate([first, second], axis=1)


def pair_then_scatter(term, axis_name):
    count = lax.axis_size(axis_name)
    block = term.shape[0] // count
    index = lax.axis_index(axis_name)
    pairs = term.reshape((count // 2, 2, block) + term.shape[1:])
    mine = index & 1
    keep = lax.dynamic_index_in_dim(pairs, mine, axis=1, keepdims=False)
    send = lax.dynamic_index_in_dim(pairs, 1 - mine, axis=1, keepdims=False)
    received = lax.ppermute(send.astype(jnp.bfloat16), axis_name, perm=[(i, i ^ 1) for i in range(count)])
    summed = (keep + received.astype(jnp.float32)).astype(jnp.bfloat16)
    groups = [list(range(low, count, 2)) for low in range(2)]
    return lax.psum_scatter(
        summed.reshape((count // 2 * block,) + term.shape[1:]),
        axis_name,
        scatter_dimension=0,
        axis_index_groups=groups,
        tiled=True,
    ).astype(jnp.float32)


def body(cells, cotangent, row_weight, col_weight):
    row_saved = forward(cells, row_weight, 1, True)
    mid_columns = lax.all_to_all(row_saved[4], "cell", split_axis=1, concat_axis=0, tiled=True)
    col_saved = forward(mid_columns, col_weight, 0, False)
    grad_mid_columns, grad_col_proj = backward(col_saved, col_weight, cotangent, 0)
    col_term = weight_term(col_saved[1], grad_col_proj, col_saved[3], cotangent, 0)
    col_grad = pair_then_scatter(col_term, "cell")
    grad_mid = lax.all_to_all(grad_mid_columns, "cell", split_axis=0, concat_axis=1, tiled=True)
    grad_cells, grad_row_proj = backward(row_saved, row_weight, grad_mid, 1)
    row_term = weight_term(row_saved[1], grad_row_proj, row_saved[3], grad_mid, 1)
    row_grad = pair_then_scatter(row_term, "cell")
    return (grad_cells, row_grad, col_grad)


def solution(mesh):
    placed = (P(("groups", "cell"), None, None), P("groups", "cell", None), P(), P())
    return jax.shard_map(
        body,
        mesh=mesh,
        in_specs=placed,
        out_specs=(
            P(("groups", "cell"), None, None),
            P(("groups", "cell"), None),
            P(("groups", "cell"), None),
        ),
        check_vma=False,
    )
```

```python
import jax
import jax.numpy as jnp
from jax import lax
from jax.sharding import PartitionSpec as P

HEADS = 12


EPS = 1e-06


def normalize(values):
    return values * lax.rsqrt(jnp.mean(values * values, axis=-1, keepdims=True) + EPS)


def attend_heads(queries, keys_part, values_part):
    head_size = queries.shape[-1]
    scores = jnp.einsum(
        "bhle,bhme->bhlm", queries, keys_part, preferred_element_type=jnp.float32
    ) * head_size ** (-0.5)
    weights = jax.nn.softmax(scores, axis=-1).astype(jnp.bfloat16)
    mixture = jnp.einsum("bhlm,bhme->bhle", weights, values_part, preferred_element_type=jnp.float32)
    return mixture.astype(jnp.bfloat16)


def forms_of(attn_dim):
    return "bld" if attn_dim == 1 else "lbd", "blf" if attn_dim == 1 else "lbf"


def split_weight(weight):
    model_width = weight.shape[0]
    head_size = model_width // HEADS
    projection = weight[:, : 3 * model_width].reshape(model_width, 3, HEADS, head_size)
    output = weight[:, 3 * model_width :].reshape(HEADS, head_size, model_width)
    return projection, output


def forward(cells_in, weight, attn_dim, with_result):
    cell_form, out_form = forms_of(attn_dim)
    projection, output = split_weight(weight)
    inputs_f = cells_in.astype(jnp.float32)
    normed = normalize(inputs_f).astype(jnp.bfloat16)
    projected = jnp.einsum(
        cell_form + ",dthe->tbhle", normed, projection, preferred_element_type=jnp.float32
    ).astype(jnp.bfloat16)
    attended = attend_heads(projected[0], projected[1], projected[2])
    result = None
    if with_result:
        result = (
            inputs_f
            + jnp.einsum("bhle,hef->" + out_form, attended, output, preferred_element_type=jnp.float32)
        ).astype(jnp.bfloat16)
    return (inputs_f, normed, projected, attended, result)


def backward(saved, weight, upstream, attn_dim):
    inputs_f, normed, projected, attended, result = saved
    cell_form, out_form = forms_of(attn_dim)
    projection, output = split_weight(weight)
    grad_attended = jnp.einsum(
        out_form + ",hef->bhle", upstream, output, preferred_element_type=jnp.float32
    ).astype(jnp.bfloat16)
    unused, pull = jax.vjp(attend_heads, projected[0], projected[1], projected[2])
    grad_projected = jnp.stack(pull(grad_attended)).astype(jnp.bfloat16)
    grad_normed = jnp.einsum(
        "tbhle,dthe->" + cell_form, grad_projected, projection, preferred_element_type=jnp.float32
    )
    unused_norm, pull_norm = jax.vjp(normalize, inputs_f)
    grad_input = (upstream.astype(jnp.float32) + pull_norm(grad_normed)[0]).astype(jnp.bfloat16)
    return (grad_input, grad_projected)


def weight_term(normed, grad_projected, attended, upstream, attn_dim):
    cell_form, out_form = forms_of(attn_dim)
    model_width = normed.shape[-1]
    first = jnp.einsum(
        cell_form + ",tbhle->dthe", normed, grad_projected, preferred_element_type=jnp.float32
    ).reshape(model_width, 3 * model_width)
    second = jnp.einsum(
        "bhle," + out_form + "->hef", attended, upstream, preferred_element_type=jnp.float32
    ).reshape(model_width, model_width)
    return jnp.concatenate([first, second], axis=1)


def pair_then_exchange(term, axis_name):
    count = lax.axis_size(axis_name)
    block = term.shape[0] // count
    index = lax.axis_index(axis_name)
    sent = lax.optimization_barrier(term.astype(jnp.bfloat16))
    pairs = sent.reshape((count // 2, 2, block) + term.shape[1:])
    mine = index & 1
    keep = lax.dynamic_index_in_dim(pairs, mine, axis=1, keepdims=False)
    send = lax.dynamic_index_in_dim(pairs, 1 - mine, axis=1, keepdims=False)
    received = lax.ppermute(send, axis_name, perm=[(i, i ^ 1) for i in range(count)])
    summed = (keep.astype(jnp.float32) + received.astype(jnp.float32)).astype(jnp.bfloat16)
    groups = [list(range(low, count, 2)) for low in range(2)]
    gathered = lax.all_to_all(
        summed, axis_name, split_axis=0, concat_axis=0, axis_index_groups=groups, tiled=True
    )
    return jnp.sum(gathered.astype(jnp.float32), axis=0)


def body(cells, cotangent, row_weight, col_weight):
    row_saved = forward(cells, row_weight, 1, True)
    mid_columns = lax.all_to_all(row_saved[4], "cell", split_axis=1, concat_axis=0, tiled=True)
    col_saved = forward(mid_columns, col_weight, 0, False)
    grad_mid_columns, grad_col_proj = backward(col_saved, col_weight, cotangent, 0)
    col_term = weight_term(col_saved[1], grad_col_proj, col_saved[3], cotangent, 0)
    col_grad = pair_then_exchange(col_term, "cell")
    grad_mid = lax.all_to_all(grad_mid_columns, "cell", split_axis=0, concat_axis=1, tiled=True)
    grad_cells, grad_row_proj = backward(row_saved, row_weight, grad_mid, 1)
    row_term = weight_term(row_saved[1], grad_row_proj, row_saved[3], grad_mid, 1)
    row_grad = lax.psum_scatter(
        row_term.astype(jnp.bfloat16), "cell", scatter_dimension=0, tiled=True
    ).astype(jnp.float32)
    return (grad_cells, row_grad, col_grad)


def solution(mesh):
    placed = (P(("groups", "cell"), None, None), P("groups", "cell", None), P(), P())
    return jax.shard_map(
        body,
        mesh=mesh,
        in_specs=placed,
        out_specs=(
            P(("groups", "cell"), None, None),
            P(("groups", "cell"), None),
            P(("groups", "cell"), None),
        ),
        check_vma=False,
    )
```

```python
import jax
import jax.numpy as jnp
from jax import lax
from jax.sharding import PartitionSpec as P

HEADS = 12


EPS = 1e-06


def normalize(values):
    return values * lax.rsqrt(jnp.mean(values * values, axis=-1, keepdims=True) + EPS)


def attend_heads(queries, keys_part, values_part):
    head_size = queries.shape[-1]
    scores = jnp.einsum(
        "bhle,bhme->bhlm", queries, keys_part, preferred_element_type=jnp.float32
    ) * head_size ** (-0.5)
    weights = jax.nn.softmax(scores, axis=-1).astype(jnp.bfloat16)
    mixture = jnp.einsum("bhlm,bhme->bhle", weights, values_part, preferred_element_type=jnp.float32)
    return mixture.astype(jnp.bfloat16)


def forms_of(attn_dim):
    return "bld" if attn_dim == 1 else "lbd", "blf" if attn_dim == 1 else "lbf"


def split_weight(weight):
    model_width = weight.shape[0]
    head_size = model_width // HEADS
    projection = weight[:, : 3 * model_width].reshape(model_width, 3, HEADS, head_size)
    output = weight[:, 3 * model_width :].reshape(HEADS, head_size, model_width)
    return projection, output


def forward(cells_in, weight, attn_dim, with_result):
    cell_form, out_form = forms_of(attn_dim)
    projection, output = split_weight(weight)
    inputs_f = cells_in.astype(jnp.float32)
    normed = normalize(inputs_f).astype(jnp.bfloat16)
    projected = jnp.einsum(
        cell_form + ",dthe->tbhle", normed, projection, preferred_element_type=jnp.float32
    ).astype(jnp.bfloat16)
    attended = attend_heads(projected[0], projected[1], projected[2])
    result = None
    if with_result:
        result = (
            inputs_f
            + jnp.einsum("bhle,hef->" + out_form, attended, output, preferred_element_type=jnp.float32)
        ).astype(jnp.bfloat16)
    return (inputs_f, normed, projected, attended, result)


def backward(saved, weight, upstream, attn_dim):
    inputs_f, normed, projected, attended, result = saved
    cell_form, out_form = forms_of(attn_dim)
    projection, output = split_weight(weight)
    grad_attended = jnp.einsum(
        out_form + ",hef->bhle", upstream, output, preferred_element_type=jnp.float32
    ).astype(jnp.bfloat16)
    unused, pull = jax.vjp(attend_heads, projected[0], projected[1], projected[2])
    grad_projected = jnp.stack(pull(grad_attended)).astype(jnp.bfloat16)
    grad_normed = jnp.einsum(
        "tbhle,dthe->" + cell_form, grad_projected, projection, preferred_element_type=jnp.float32
    )
    unused_norm, pull_norm = jax.vjp(normalize, inputs_f)
    grad_input = (upstream.astype(jnp.float32) + pull_norm(grad_normed)[0]).astype(jnp.bfloat16)
    return (grad_input, grad_projected)


def weight_term(normed, grad_projected, attended, upstream, attn_dim):
    cell_form, out_form = forms_of(attn_dim)
    model_width = normed.shape[-1]
    first = jnp.einsum(
        cell_form + ",tbhle->dthe", normed, grad_projected, preferred_element_type=jnp.float32
    ).reshape(model_width, 3 * model_width)
    second = jnp.einsum(
        "bhle," + out_form + "->hef", attended, upstream, preferred_element_type=jnp.float32
    ).reshape(model_width, model_width)
    return jnp.concatenate([first, second], axis=1)


def pair_presum(term, axis_name):
    count = lax.axis_size(axis_name)
    block = term.shape[0] // count
    index = lax.axis_index(axis_name)
    sent = lax.optimization_barrier(term.astype(jnp.bfloat16))
    pairs = sent.reshape((count // 2, 2, block) + term.shape[1:])
    mine = index & 1
    keep = lax.dynamic_index_in_dim(pairs, mine, axis=1, keepdims=False)
    send = lax.dynamic_index_in_dim(pairs, 1 - mine, axis=1, keepdims=False)
    received = lax.ppermute(send, axis_name, perm=[(i, i ^ 1) for i in range(count)])
    return (keep.astype(jnp.float32) + received.astype(jnp.float32)).astype(jnp.bfloat16)


def exchange_blocks(summed, axis_name):
    count = lax.axis_size(axis_name)
    groups = [list(range(low, count, 2)) for low in range(2)]
    gathered = lax.all_to_all(
        summed, axis_name, split_axis=0, concat_axis=0, axis_index_groups=groups, tiled=True
    )
    return jnp.sum(gathered.astype(jnp.float32), axis=0)


def body(cells, cotangent, row_weight, col_weight):
    row_saved = forward(cells, row_weight, 1, True)
    mid_columns = lax.all_to_all(row_saved[4], "cell", split_axis=1, concat_axis=0, tiled=True)
    col_saved = forward(mid_columns, col_weight, 0, False)
    grad_mid_columns, grad_col_proj = backward(col_saved, col_weight, cotangent, 0)
    col_term = weight_term(col_saved[1], grad_col_proj, col_saved[3], cotangent, 0)
    col_summed = pair_presum(col_term, "cell")
    grad_mid = lax.all_to_all(grad_mid_columns, "cell", split_axis=0, concat_axis=1, tiled=True)
    col_summed, grad_mid = lax.optimization_barrier((col_summed, grad_mid))
    col_grad = exchange_blocks(col_summed, "cell")
    grad_cells, grad_row_proj = backward(row_saved, row_weight, grad_mid, 1)
    row_term = weight_term(row_saved[1], grad_row_proj, row_saved[3], grad_mid, 1)
    row_grad = exchange_blocks(pair_presum(row_term, "cell"), "cell")
    return (grad_cells, row_grad, col_grad)


def solution(mesh):
    placed = (P(("groups", "cell"), None, None), P("groups", "cell", None), P(), P())
    return jax.shard_map(
        body,
        mesh=mesh,
        in_specs=placed,
        out_specs=(
            P(("groups", "cell"), None, None),
            P(("groups", "cell"), None),
            P(("groups", "cell"), None),
        ),
        check_vma=False,
    )
```

```python
import jax
import jax.numpy as jnp
from jax import lax
from jax.sharding import PartitionSpec as P

HEADS = 12


EPS = 1e-06


def normalize(values):
    return values * lax.rsqrt(jnp.mean(values * values, axis=-1, keepdims=True) + EPS)


def attend_heads(queries, keys_part, values_part):
    head_size = queries.shape[-1]
    scores = jnp.einsum(
        "bhle,bhme->bhlm", queries, keys_part, preferred_element_type=jnp.float32
    ) * head_size ** (-0.5)
    weights = jax.nn.softmax(scores, axis=-1).astype(jnp.bfloat16)
    mixture = jnp.einsum("bhlm,bhme->bhle", weights, values_part, preferred_element_type=jnp.float32)
    return mixture.astype(jnp.bfloat16)


def forms_of(attn_dim):
    return "bld" if attn_dim == 1 else "lbd", "blf" if attn_dim == 1 else "lbf"


def split_weight(weight):
    model_width = weight.shape[0]
    head_size = model_width // HEADS
    projection = weight[:, : 3 * model_width].reshape(model_width, 3, HEADS, head_size)
    output = weight[:, 3 * model_width :].reshape(HEADS, head_size, model_width)
    return projection, output


def forward(cells_in, weight, attn_dim, with_result):
    cell_form, out_form = forms_of(attn_dim)
    projection, output = split_weight(weight)
    inputs_f = cells_in.astype(jnp.float32)
    normed = normalize(inputs_f).astype(jnp.bfloat16)
    projected = jnp.einsum(
        cell_form + ",dthe->tbhle", normed, projection, preferred_element_type=jnp.float32
    ).astype(jnp.bfloat16)
    attended = attend_heads(projected[0], projected[1], projected[2])
    result = None
    if with_result:
        result = (
            inputs_f
            + jnp.einsum("bhle,hef->" + out_form, attended, output, preferred_element_type=jnp.float32)
        ).astype(jnp.bfloat16)
    return (inputs_f, normed, projected, attended, result)


def backward(saved, weight, upstream, attn_dim):
    inputs_f, normed, projected, attended, result = saved
    cell_form, out_form = forms_of(attn_dim)
    projection, output = split_weight(weight)
    grad_attended = jnp.einsum(
        out_form + ",hef->bhle", upstream, output, preferred_element_type=jnp.float32
    ).astype(jnp.bfloat16)
    unused, pull = jax.vjp(attend_heads, projected[0], projected[1], projected[2])
    grad_projected = jnp.stack(pull(grad_attended)).astype(jnp.bfloat16)
    grad_normed = jnp.einsum(
        "tbhle,dthe->" + cell_form, grad_projected, projection, preferred_element_type=jnp.float32
    )
    unused_norm, pull_norm = jax.vjp(normalize, inputs_f)
    grad_input = (upstream.astype(jnp.float32) + pull_norm(grad_normed)[0]).astype(jnp.bfloat16)
    return (grad_input, grad_projected)


def weight_term(normed, grad_projected, attended, upstream, attn_dim):
    cell_form, out_form = forms_of(attn_dim)
    model_width = normed.shape[-1]
    first = jnp.einsum(
        cell_form + ",tbhle->dthe", normed, grad_projected, preferred_element_type=jnp.float32
    ).reshape(model_width, 3 * model_width)
    second = jnp.einsum(
        "bhle," + out_form + "->hef", attended, upstream, preferred_element_type=jnp.float32
    ).reshape(model_width, model_width)
    return jnp.concatenate([first, second], axis=1)


def pair_presum(term, axis_name):
    count = lax.axis_size(axis_name)
    block = term.shape[0] // count
    index = lax.axis_index(axis_name)
    sent = lax.optimization_barrier(term.astype(jnp.bfloat16))
    pairs = sent.reshape((count // 2, 2, block) + term.shape[1:])
    couples = [[low, low + 1] for low in range(0, count, 2)]
    swapped = lax.all_to_all(pairs, axis_name, split_axis=1, concat_axis=1, axis_index_groups=couples, tiled=True)
    return jnp.sum(swapped.astype(jnp.float32), axis=1).astype(jnp.bfloat16)


def exchange_blocks(summed, axis_name):
    count = lax.axis_size(axis_name)
    groups = [list(range(low, count, 2)) for low in range(2)]
    gathered = lax.all_to_all(
        summed, axis_name, split_axis=0, concat_axis=0, axis_index_groups=groups, tiled=True
    )
    return jnp.sum(gathered.astype(jnp.float32), axis=0)


def body(cells, cotangent, row_weight, col_weight):
    row_saved = forward(cells, row_weight, 1, True)
    mid_columns = lax.all_to_all(row_saved[4], "cell", split_axis=1, concat_axis=0, tiled=True)
    col_saved = forward(mid_columns, col_weight, 0, False)
    grad_mid_columns, grad_col_proj = backward(col_saved, col_weight, cotangent, 0)
    col_term = weight_term(col_saved[1], grad_col_proj, col_saved[3], cotangent, 0)
    col_grad = lax.psum_scatter(
        col_term.astype(jnp.bfloat16), "cell", scatter_dimension=0, tiled=True
    ).astype(jnp.float32)
    grad_mid = lax.all_to_all(grad_mid_columns, "cell", split_axis=0, concat_axis=1, tiled=True)
    grad_cells, grad_row_proj = backward(row_saved, row_weight, grad_mid, 1)
    row_term = weight_term(row_saved[1], grad_row_proj, row_saved[3], grad_mid, 1)
    row_grad = exchange_blocks(pair_presum(row_term, "cell"), "cell")
    return (grad_cells, row_grad, col_grad)


def solution(mesh):
    placed = (P(("groups", "cell"), None, None), P("groups", "cell", None), P(), P())
    return jax.shard_map(
        body,
        mesh=mesh,
        in_specs=placed,
        out_specs=(
            P(("groups", "cell"), None, None),
            P(("groups", "cell"), None),
            P(("groups", "cell"), None),
        ),
        check_vma=False,
    )
```

```python
import jax
import jax.numpy as jnp
from jax import lax
from jax.sharding import PartitionSpec as P

HEADS = 12


EPS = 1e-06


def normalize(values):
    return values * lax.rsqrt(jnp.mean(values * values, axis=-1, keepdims=True) + EPS)


def attend_heads(queries, keys_part, values_part):
    head_size = queries.shape[-1]
    scores = jnp.einsum(
        "bhle,bhme->bhlm", queries, keys_part, preferred_element_type=jnp.float32
    ) * head_size ** (-0.5)
    weights = jax.nn.softmax(scores, axis=-1).astype(jnp.bfloat16)
    mixture = jnp.einsum("bhlm,bhme->bhle", weights, values_part, preferred_element_type=jnp.float32)
    return mixture.astype(jnp.bfloat16)


def forms_of(attn_dim):
    return "bld" if attn_dim == 1 else "lbd", "blf" if attn_dim == 1 else "lbf"


def split_weight(weight):
    model_width = weight.shape[0]
    head_size = model_width // HEADS
    projection = weight[:, : 3 * model_width].reshape(model_width, 3, HEADS, head_size)
    output = weight[:, 3 * model_width :].reshape(HEADS, head_size, model_width)
    return projection, output


def forward(cells_in, weight, attn_dim, with_result):
    cell_form, out_form = forms_of(attn_dim)
    projection, output = split_weight(weight)
    inputs_f = cells_in.astype(jnp.float32)
    normed = normalize(inputs_f).astype(jnp.bfloat16)
    projected = jnp.einsum(
        cell_form + ",dthe->tbhle", normed, projection, preferred_element_type=jnp.float32
    ).astype(jnp.bfloat16)
    attended = attend_heads(projected[0], projected[1], projected[2])
    result = None
    if with_result:
        result = (
            inputs_f
            + jnp.einsum("bhle,hef->" + out_form, attended, output, preferred_element_type=jnp.float32)
        ).astype(jnp.bfloat16)
    return (inputs_f, normed, projected, attended, result)


def backward(saved, weight, upstream, attn_dim):
    inputs_f, normed, projected, attended, result = saved
    cell_form, out_form = forms_of(attn_dim)
    projection, output = split_weight(weight)
    grad_attended = jnp.einsum(
        out_form + ",hef->bhle", upstream, output, preferred_element_type=jnp.float32
    ).astype(jnp.bfloat16)
    unused, pull = jax.vjp(attend_heads, projected[0], projected[1], projected[2])
    grad_projected = jnp.stack(pull(grad_attended)).astype(jnp.bfloat16)
    grad_normed = jnp.einsum(
        "tbhle,dthe->" + cell_form, grad_projected, projection, preferred_element_type=jnp.float32
    )
    unused_norm, pull_norm = jax.vjp(normalize, inputs_f)
    grad_input = (upstream.astype(jnp.float32) + pull_norm(grad_normed)[0]).astype(jnp.bfloat16)
    return (grad_input, grad_projected)


def weight_term(normed, grad_projected, attended, upstream, attn_dim):
    cell_form, out_form = forms_of(attn_dim)
    model_width = normed.shape[-1]
    first = jnp.einsum(
        cell_form + ",tbhle->dthe", normed, grad_projected, preferred_element_type=jnp.float32
    ).reshape(model_width, 3 * model_width)
    second = jnp.einsum(
        "bhle," + out_form + "->hef", attended, upstream, preferred_element_type=jnp.float32
    ).reshape(model_width, model_width)
    return jnp.concatenate([first, second], axis=1)


def pair_presum(term, axis_name):
    count = lax.axis_size(axis_name)
    block = term.shape[0] // count
    index = lax.axis_index(axis_name)
    sent = lax.optimization_barrier(term.astype(jnp.bfloat16))
    pairs = jnp.swapaxes(sent.reshape((count // 2, 2, block) + term.shape[1:]), 0, 1)
    couples = [[low, low + 1] for low in range(0, count, 2)]
    swapped = lax.all_to_all(pairs, axis_name, split_axis=0, concat_axis=0, axis_index_groups=couples, tiled=True)
    return (swapped[0].astype(jnp.float32) + swapped[1].astype(jnp.float32)).astype(jnp.bfloat16)


def exchange_blocks(summed, axis_name):
    count = lax.axis_size(axis_name)
    groups = [list(range(low, count, 2)) for low in range(2)]
    gathered = lax.all_to_all(
        summed, axis_name, split_axis=0, concat_axis=0, axis_index_groups=groups, tiled=True
    )
    return jnp.sum(gathered.astype(jnp.float32), axis=0)


def body(cells, cotangent, row_weight, col_weight):
    row_saved = forward(cells, row_weight, 1, True)
    mid_columns = lax.all_to_all(row_saved[4], "cell", split_axis=1, concat_axis=0, tiled=True)
    col_saved = forward(mid_columns, col_weight, 0, False)
    grad_mid_columns, grad_col_proj = backward(col_saved, col_weight, cotangent, 0)
    col_term = weight_term(col_saved[1], grad_col_proj, col_saved[3], cotangent, 0)
    col_grad = lax.psum_scatter(
        col_term.astype(jnp.bfloat16), "cell", scatter_dimension=0, tiled=True
    ).astype(jnp.float32)
    grad_mid = lax.all_to_all(grad_mid_columns, "cell", split_axis=0, concat_axis=1, tiled=True)
    grad_cells, grad_row_proj = backward(row_saved, row_weight, grad_mid, 1)
    row_term = weight_term(row_saved[1], grad_row_proj, row_saved[3], grad_mid, 1)
    row_grad = exchange_blocks(pair_presum(row_term, "cell"), "cell")
    return (grad_cells, row_grad, col_grad)


def solution(mesh):
    placed = (P(("groups", "cell"), None, None), P("groups", "cell", None), P(), P())
    return jax.shard_map(
        body,
        mesh=mesh,
        in_specs=placed,
        out_specs=(
            P(("groups", "cell"), None, None),
            P(("groups", "cell"), None),
            P(("groups", "cell"), None),
        ),
        check_vma=False,
    )
```

```python
import jax
import jax.numpy as jnp
from jax import lax
from jax.sharding import PartitionSpec as P

HEADS = 12


EPS = 1e-06


def normalize(values):
    return values * lax.rsqrt(jnp.mean(values * values, axis=-1, keepdims=True) + EPS)


def attend_heads(queries, keys_part, values_part):
    head_size = queries.shape[-1]
    scores = jnp.einsum(
        "bhle,bhme->bhlm", queries, keys_part, preferred_element_type=jnp.float32
    ) * head_size ** (-0.5)
    weights = jax.nn.softmax(scores, axis=-1).astype(jnp.bfloat16)
    mixture = jnp.einsum("bhlm,bhme->bhle", weights, values_part, preferred_element_type=jnp.float32)
    return mixture.astype(jnp.bfloat16)


def forms_of(attn_dim):
    return "bld" if attn_dim == 1 else "lbd", "blf" if attn_dim == 1 else "lbf"


def split_weight(weight):
    model_width = weight.shape[0]
    head_size = model_width // HEADS
    projection = weight[:, : 3 * model_width].reshape(model_width, 3, HEADS, head_size)
    output = weight[:, 3 * model_width :].reshape(HEADS, head_size, model_width)
    return projection, output


def forward(cells_in, weight, attn_dim, with_result):
    cell_form, out_form = forms_of(attn_dim)
    projection, output = split_weight(weight)
    inputs_f = cells_in.astype(jnp.float32)
    normed = normalize(inputs_f).astype(jnp.bfloat16)
    projected = jnp.einsum(
        cell_form + ",dthe->tbhle", normed, projection, preferred_element_type=jnp.float32
    ).astype(jnp.bfloat16)
    attended = attend_heads(projected[0], projected[1], projected[2])
    result = None
    if with_result:
        result = (
            inputs_f
            + jnp.einsum("bhle,hef->" + out_form, attended, output, preferred_element_type=jnp.float32)
        ).astype(jnp.bfloat16)
    return (inputs_f, normed, projected, attended, result)


def backward(saved, weight, upstream, attn_dim):
    inputs_f, normed, projected, attended, result = saved
    cell_form, out_form = forms_of(attn_dim)
    projection, output = split_weight(weight)
    grad_attended = jnp.einsum(
        out_form + ",hef->bhle", upstream, output, preferred_element_type=jnp.float32
    ).astype(jnp.bfloat16)
    unused, pull = jax.vjp(attend_heads, projected[0], projected[1], projected[2])
    grad_projected = jnp.stack(pull(grad_attended)).astype(jnp.bfloat16)
    grad_normed = jnp.einsum(
        "tbhle,dthe->" + cell_form, grad_projected, projection, preferred_element_type=jnp.float32
    )
    unused_norm, pull_norm = jax.vjp(normalize, inputs_f)
    grad_input = (upstream.astype(jnp.float32) + pull_norm(grad_normed)[0]).astype(jnp.bfloat16)
    return (grad_input, grad_projected)


def weight_term(normed, grad_projected, attended, upstream, attn_dim):
    cell_form, out_form = forms_of(attn_dim)
    model_width = normed.shape[-1]
    first = jnp.einsum(
        cell_form + ",tbhle->dthe", normed, grad_projected, preferred_element_type=jnp.float32
    ).reshape(model_width, 3 * model_width)
    second = jnp.einsum(
        "bhle," + out_form + "->hef", attended, upstream, preferred_element_type=jnp.float32
    ).reshape(model_width, model_width)
    return jnp.concatenate([first, second], axis=1)


def swap_sum(parts, axis_name, groups):
    received = lax.all_to_all(parts, axis_name, split_axis=0, concat_axis=0, axis_index_groups=groups, tiled=True)
    total = received[0].astype(jnp.float32)
    for part in range(1, received.shape[0]):
        total = total + received[part].astype(jnp.float32)
    return total


def staged_scatter(term, axis_name):
    count = lax.axis_size(axis_name)
    if count % 4:
        return lax.psum_scatter(
            term.astype(jnp.bfloat16), axis_name, scatter_dimension=0, tiled=True
        ).astype(jnp.float32)
    block = term.shape[0] // count
    rest = term.shape[1:]
    sent = lax.optimization_barrier(term.astype(jnp.bfloat16))
    blocks = sent.reshape((count // 4, 2, 2, block) + rest)
    couples = [[low, low + 1] for low in range(0, count, 2)]
    first = swap_sum(jnp.moveaxis(blocks, 2, 0), axis_name, couples).astype(jnp.bfloat16)
    neighbours = [[low, low + 2] for low in range(count) if not (low >> 1) & 1]
    second = swap_sum(jnp.moveaxis(first, 1, 0), axis_name, neighbours).astype(jnp.bfloat16)
    others = [[high * 4 + low for high in range(count // 4)] for low in range(4)]
    return swap_sum(second, axis_name, others)


def body(cells, cotangent, row_weight, col_weight):
    row_saved = forward(cells, row_weight, 1, True)
    mid_columns = lax.all_to_all(row_saved[4], "cell", split_axis=1, concat_axis=0, tiled=True)
    col_saved = forward(mid_columns, col_weight, 0, False)
    grad_mid_columns, grad_col_proj = backward(col_saved, col_weight, cotangent, 0)
    col_term = weight_term(col_saved[1], grad_col_proj, col_saved[3], cotangent, 0)
    col_grad = lax.psum_scatter(
        col_term.astype(jnp.bfloat16), "cell", scatter_dimension=0, tiled=True
    ).astype(jnp.float32)
    grad_mid = lax.all_to_all(grad_mid_columns, "cell", split_axis=0, concat_axis=1, tiled=True)
    grad_cells, grad_row_proj = backward(row_saved, row_weight, grad_mid, 1)
    row_term = weight_term(row_saved[1], grad_row_proj, row_saved[3], grad_mid, 1)
    row_grad = staged_scatter(row_term, "cell")
    return (grad_cells, row_grad, col_grad)


def solution(mesh):
    placed = (P(("groups", "cell"), None, None), P("groups", "cell", None), P(), P())
    return jax.shard_map(
        body,
        mesh=mesh,
        in_specs=placed,
        out_specs=(
            P(("groups", "cell"), None, None),
            P(("groups", "cell"), None),
            P(("groups", "cell"), None),
        ),
        check_vma=False,
    )
```

```python
import jax
import jax.numpy as jnp
from jax import lax
from jax.sharding import PartitionSpec as P

HEADS = 12


EPS = 1e-06


def normalize(values):
    return values * lax.rsqrt(jnp.mean(values * values, axis=-1, keepdims=True) + EPS)


def attend_heads(queries, keys_part, values_part):
    head_size = queries.shape[-1]
    scores = jnp.einsum(
        "bhle,bhme->bhlm", queries, keys_part, preferred_element_type=jnp.float32
    ) * head_size ** (-0.5)
    weights = jax.nn.softmax(scores, axis=-1).astype(jnp.bfloat16)
    mixture = jnp.einsum("bhlm,bhme->bhle", weights, values_part, preferred_element_type=jnp.float32)
    return mixture.astype(jnp.bfloat16)


def forms_of(attn_dim):
    return "bld" if attn_dim == 1 else "lbd", "blf" if attn_dim == 1 else "lbf"


def split_weight(weight):
    model_width = weight.shape[0]
    head_size = model_width // HEADS
    projection = weight[:, : 3 * model_width].reshape(model_width, 3, HEADS, head_size)
    output = weight[:, 3 * model_width :].reshape(HEADS, head_size, model_width)
    return projection, output


def forward(cells_in, weight, attn_dim, with_result):
    cell_form, out_form = forms_of(attn_dim)
    projection, output = split_weight(weight)
    inputs_f = cells_in.astype(jnp.float32)
    normed = normalize(inputs_f).astype(jnp.bfloat16)
    projected = jnp.einsum(
        cell_form + ",dthe->tbhle", normed, projection, preferred_element_type=jnp.float32
    ).astype(jnp.bfloat16)
    attended = attend_heads(projected[0], projected[1], projected[2])
    result = None
    if with_result:
        result = (
            inputs_f
            + jnp.einsum("bhle,hef->" + out_form, attended, output, preferred_element_type=jnp.float32)
        ).astype(jnp.bfloat16)
    return (inputs_f, normed, projected, attended, result)


def backward(saved, weight, upstream, attn_dim):
    inputs_f, normed, projected, attended, result = saved
    cell_form, out_form = forms_of(attn_dim)
    projection, output = split_weight(weight)
    grad_attended = jnp.einsum(
        out_form + ",hef->bhle", upstream, output, preferred_element_type=jnp.float32
    ).astype(jnp.bfloat16)
    unused, pull = jax.vjp(attend_heads, projected[0], projected[1], projected[2])
    grad_projected = jnp.stack(pull(grad_attended)).astype(jnp.bfloat16)
    grad_normed = jnp.einsum(
        "tbhle,dthe->" + cell_form, grad_projected, projection, preferred_element_type=jnp.float32
    )
    unused_norm, pull_norm = jax.vjp(normalize, inputs_f)
    grad_input = (upstream.astype(jnp.float32) + pull_norm(grad_normed)[0]).astype(jnp.bfloat16)
    return (grad_input, grad_projected)


def weight_term(normed, grad_projected, attended, upstream, attn_dim):
    cell_form, out_form = forms_of(attn_dim)
    model_width = normed.shape[-1]
    first = jnp.einsum(
        cell_form + ",tbhle->dthe", normed, grad_projected, preferred_element_type=jnp.float32
    ).reshape(model_width, 3 * model_width)
    second = jnp.einsum(
        "bhle," + out_form + "->hef", attended, upstream, preferred_element_type=jnp.float32
    ).reshape(model_width, model_width)
    return jnp.concatenate([first, second], axis=1)


def swap_sum(parts, axis_name, groups):
    received = lax.all_to_all(parts, axis_name, split_axis=0, concat_axis=0, axis_index_groups=groups, tiled=True)
    total = received[0].astype(jnp.float32)
    for part in range(1, received.shape[0]):
        total = total + received[part].astype(jnp.float32)
    return total


def staged_scatter(term, axis_name):
    count = lax.axis_size(axis_name)
    if count % 4:
        return lax.psum_scatter(
            term.astype(jnp.bfloat16), axis_name, scatter_dimension=0, tiled=True
        ).astype(jnp.float32)
    block = term.shape[0] // count
    rest = term.shape[1:]
    sent = lax.optimization_barrier(term.astype(jnp.bfloat16))
    blocks = sent.reshape((count // 4, 2, 2, block) + rest)
    couples = [[low, low + 1] for low in range(0, count, 2)]
    first = swap_sum(jnp.moveaxis(blocks, 2, 0), axis_name, couples)
    index = lax.axis_index(axis_name)
    mine = (index >> 1) & 1
    keep = lax.dynamic_index_in_dim(first, mine, axis=1, keepdims=False)
    send = lax.dynamic_index_in_dim(first, 1 - mine, axis=1, keepdims=False)
    received = lax.ppermute(send.astype(jnp.bfloat16), axis_name, perm=[(i, i ^ 2) for i in range(count)])
    second = (keep + received.astype(jnp.float32)).astype(jnp.bfloat16)
    others = [[high * 4 + low for high in range(count // 4)] for low in range(4)]
    return swap_sum(second, axis_name, others)


def body(cells, cotangent, row_weight, col_weight):
    row_saved = forward(cells, row_weight, 1, True)
    mid_columns = lax.all_to_all(row_saved[4], "cell", split_axis=1, concat_axis=0, tiled=True)
    col_saved = forward(mid_columns, col_weight, 0, False)
    grad_mid_columns, grad_col_proj = backward(col_saved, col_weight, cotangent, 0)
    col_term = weight_term(col_saved[1], grad_col_proj, col_saved[3], cotangent, 0)
    col_grad = lax.psum_scatter(
        col_term.astype(jnp.bfloat16), "cell", scatter_dimension=0, tiled=True
    ).astype(jnp.float32)
    grad_mid = lax.all_to_all(grad_mid_columns, "cell", split_axis=0, concat_axis=1, tiled=True)
    grad_cells, grad_row_proj = backward(row_saved, row_weight, grad_mid, 1)
    row_term = weight_term(row_saved[1], grad_row_proj, row_saved[3], grad_mid, 1)
    row_grad = staged_scatter(row_term, "cell")
    return (grad_cells, row_grad, col_grad)


def solution(mesh):
    placed = (P(("groups", "cell"), None, None), P("groups", "cell", None), P(), P())
    return jax.shard_map(
        body,
        mesh=mesh,
        in_specs=placed,
        out_specs=(
            P(("groups", "cell"), None, None),
            P(("groups", "cell"), None),
            P(("groups", "cell"), None),
        ),
        check_vma=False,
    )
```

```python
import jax
import jax.numpy as jnp
from jax import lax
from jax.sharding import PartitionSpec as P

HEADS = 12


EPS = 1e-06


def normalize(values):
    return values * lax.rsqrt(jnp.mean(values * values, axis=-1, keepdims=True) + EPS)


def attend_heads(queries, keys_part, values_part):
    head_size = queries.shape[-1]
    scores = jnp.einsum(
        "bhle,bhme->bhlm", queries, keys_part, preferred_element_type=jnp.float32
    ) * head_size ** (-0.5)
    weights = jax.nn.softmax(scores, axis=-1).astype(jnp.bfloat16)
    mixture = jnp.einsum("bhlm,bhme->bhle", weights, values_part, preferred_element_type=jnp.float32)
    return mixture.astype(jnp.bfloat16)


def forms_of(attn_dim):
    return "bld" if attn_dim == 1 else "lbd", "blf" if attn_dim == 1 else "lbf"


def split_weight(weight):
    model_width = weight.shape[0]
    head_size = model_width // HEADS
    projection = weight[:, : 3 * model_width].reshape(model_width, 3, HEADS, head_size)
    output = weight[:, 3 * model_width :].reshape(HEADS, head_size, model_width)
    return projection, output


def forward(cells_in, weight, attn_dim, with_result):
    cell_form, out_form = forms_of(attn_dim)
    projection, output = split_weight(weight)
    inputs_f = cells_in.astype(jnp.float32)
    normed = normalize(inputs_f).astype(jnp.bfloat16)
    projected = jnp.einsum(
        cell_form + ",dthe->tbhle", normed, projection, preferred_element_type=jnp.float32
    ).astype(jnp.bfloat16)
    attended = attend_heads(projected[0], projected[1], projected[2])
    result = None
    if with_result:
        result = (
            inputs_f
            + jnp.einsum("bhle,hef->" + out_form, attended, output, preferred_element_type=jnp.float32)
        ).astype(jnp.bfloat16)
    return (inputs_f, normed, projected, attended, result)


def backward(saved, weight, upstream, attn_dim):
    inputs_f, normed, projected, attended, result = saved
    cell_form, out_form = forms_of(attn_dim)
    projection, output = split_weight(weight)
    grad_attended = jnp.einsum(
        out_form + ",hef->bhle", upstream, output, preferred_element_type=jnp.float32
    ).astype(jnp.bfloat16)
    unused, pull = jax.vjp(attend_heads, projected[0], projected[1], projected[2])
    grad_projected = jnp.stack(pull(grad_attended)).astype(jnp.bfloat16)
    grad_normed = jnp.einsum(
        "tbhle,dthe->" + cell_form, grad_projected, projection, preferred_element_type=jnp.float32
    )
    unused_norm, pull_norm = jax.vjp(normalize, inputs_f)
    grad_input = (upstream.astype(jnp.float32) + pull_norm(grad_normed)[0]).astype(jnp.bfloat16)
    return (grad_input, grad_projected)


def weight_term(normed, grad_projected, attended, upstream, attn_dim):
    cell_form, out_form = forms_of(attn_dim)
    model_width = normed.shape[-1]
    first = jnp.einsum(
        cell_form + ",tbhle->dthe", normed, grad_projected, preferred_element_type=jnp.float32
    ).reshape(model_width, 3 * model_width)
    second = jnp.einsum(
        "bhle," + out_form + "->hef", attended, upstream, preferred_element_type=jnp.float32
    ).reshape(model_width, model_width)
    return [first, second]


def swap_sum(parts, axis_name, groups):
    received = lax.all_to_all(parts, axis_name, split_axis=0, concat_axis=0, axis_index_groups=groups, tiled=True)
    total = received[0].astype(jnp.float32)
    for part in range(1, received.shape[0]):
        total = total + received[part].astype(jnp.float32)
    return total


def row_blocks(normed, grad_projected, attended, upstream, count):
    model_width = normed.shape[-1]
    block = model_width // count
    split = normed.shape[:-1] + (count // 4, 2, 2, block)
    first = jnp.einsum(
        "blkyzr,tbhle->zkyrthe", normed.reshape(split), grad_projected, preferred_element_type=jnp.float32
    ).astype(jnp.bfloat16)
    second = jnp.einsum(
        "bhle,blf->hef", attended, upstream, preferred_element_type=jnp.float32
    ).astype(jnp.bfloat16).reshape((count // 4, 2, 2, block, model_width))
    first = first.reshape(first.shape[:4] + (3 * model_width,))
    return jnp.concatenate([first, jnp.moveaxis(second, 2, 0)], axis=-1)


def staged_scatter(term, axis_name):
    count = lax.axis_size(axis_name)
    couples = [[low, low + 1] for low in range(0, count, 2)]
    first = swap_sum(term, axis_name, couples).astype(jnp.bfloat16)
    neighbours = [[low, low + 2] for low in range(count) if not (low >> 1) & 1]
    second = swap_sum(jnp.moveaxis(first, 1, 0), axis_name, neighbours).astype(jnp.bfloat16)
    others = [[high * 4 + low for high in range(count // 4)] for low in range(4)]
    return swap_sum(second, axis_name, others)


def body(cells, cotangent, row_weight, col_weight):
    row_saved = forward(cells, row_weight, 1, True)
    mid_columns = lax.all_to_all(row_saved[4], "cell", split_axis=1, concat_axis=0, tiled=True)
    col_saved = forward(mid_columns, col_weight, 0, False)
    grad_mid_columns, grad_col_proj = backward(col_saved, col_weight, cotangent, 0)
    col_term = jnp.concatenate(weight_term(col_saved[1], grad_col_proj, col_saved[3], cotangent, 0), axis=1)
    col_grad = lax.psum_scatter(
        col_term.astype(jnp.bfloat16), "cell", scatter_dimension=0, tiled=True
    ).astype(jnp.float32)
    grad_mid = lax.all_to_all(grad_mid_columns, "cell", split_axis=0, concat_axis=1, tiled=True)
    grad_cells, grad_row_proj = backward(row_saved, row_weight, grad_mid, 1)
    count = lax.axis_size("cell")
    if count % 4:
        row_term = jnp.concatenate(weight_term(row_saved[1], grad_row_proj, row_saved[3], grad_mid, 1), axis=1)
        row_grad = lax.psum_scatter(
            row_term.astype(jnp.bfloat16), "cell", scatter_dimension=0, tiled=True
        ).astype(jnp.float32)
    else:
        row_term = row_blocks(row_saved[1], grad_row_proj, row_saved[3], grad_mid, count)
        row_grad = staged_scatter(row_term, "cell")
    return (grad_cells, row_grad, col_grad)


def solution(mesh):
    placed = (P(("groups", "cell"), None, None), P("groups", "cell", None), P(), P())
    return jax.shard_map(
        body,
        mesh=mesh,
        in_specs=placed,
        out_specs=(
            P(("groups", "cell"), None, None),
            P(("groups", "cell"), None),
            P(("groups", "cell"), None),
        ),
        check_vma=False,
    )
```

```python
import jax
import jax.numpy as jnp
from jax import lax
from jax.sharding import PartitionSpec as P

HEADS = 12


EPS = 1e-06


def normalize(values):
    return values * lax.rsqrt(jnp.mean(values * values, axis=-1, keepdims=True) + EPS)


def attend_heads(queries, keys_part, values_part):
    head_size = queries.shape[-1]
    scores = jnp.einsum(
        "bhle,bhme->bhlm", queries, keys_part, preferred_element_type=jnp.float32
    ) * head_size ** (-0.5)
    weights = jax.nn.softmax(scores, axis=-1).astype(jnp.bfloat16)
    mixture = jnp.einsum("bhlm,bhme->bhle", weights, values_part, preferred_element_type=jnp.float32)
    return mixture.astype(jnp.bfloat16)


def forms_of(attn_dim):
    return "bld" if attn_dim == 1 else "lbd", "blf" if attn_dim == 1 else "lbf"


def split_weight(weight):
    model_width = weight.shape[0]
    head_size = model_width // HEADS
    projection = weight[:, : 3 * model_width].reshape(model_width, 3, HEADS, head_size)
    output = weight[:, 3 * model_width :].reshape(HEADS, head_size, model_width)
    return projection, output


def forward(cells_in, weight, attn_dim, with_result):
    cell_form, out_form = forms_of(attn_dim)
    projection, output = split_weight(weight)
    inputs_f = cells_in.astype(jnp.float32)
    normed = normalize(inputs_f).astype(jnp.bfloat16)
    projected = jnp.einsum(
        cell_form + ",dthe->tbhle", normed, projection, preferred_element_type=jnp.float32
    ).astype(jnp.bfloat16)
    attended = attend_heads(projected[0], projected[1], projected[2])
    result = None
    if with_result:
        result = (
            inputs_f
            + jnp.einsum("bhle,hef->" + out_form, attended, output, preferred_element_type=jnp.float32)
        ).astype(jnp.bfloat16)
    return (inputs_f, normed, projected, attended, result)


def backward(saved, weight, upstream, attn_dim):
    inputs_f, normed, projected, attended, result = saved
    cell_form, out_form = forms_of(attn_dim)
    projection, output = split_weight(weight)
    grad_attended = jnp.einsum(
        out_form + ",hef->bhle", upstream, output, preferred_element_type=jnp.float32
    ).astype(jnp.bfloat16)
    unused, pull = jax.vjp(attend_heads, projected[0], projected[1], projected[2])
    grad_projected = jnp.stack(pull(grad_attended)).astype(jnp.bfloat16)
    grad_normed = jnp.einsum(
        "tbhle,dthe->" + cell_form, grad_projected, projection, preferred_element_type=jnp.float32
    )
    unused_norm, pull_norm = jax.vjp(normalize, inputs_f)
    grad_input = (upstream.astype(jnp.float32) + pull_norm(grad_normed)[0]).astype(jnp.bfloat16)
    return (grad_input, grad_projected)


def weight_term(normed, grad_projected, attended, upstream, attn_dim):
    cell_form, out_form = forms_of(attn_dim)
    model_width = normed.shape[-1]
    first = jnp.einsum(
        cell_form + ",tbhle->dthe", normed, grad_projected, preferred_element_type=jnp.float32
    ).reshape(model_width, 3 * model_width)
    second = jnp.einsum(
        "bhle," + out_form + "->hef", attended, upstream, preferred_element_type=jnp.float32
    ).reshape(model_width, model_width)
    return [first, second]


def swap_sum(parts, axis_name, groups):
    received = lax.all_to_all(parts, axis_name, split_axis=0, concat_axis=0, axis_index_groups=groups, tiled=True)
    total = received[0].astype(jnp.float32)
    for part in range(1, received.shape[0]):
        total = total + received[part].astype(jnp.float32)
    return total


def staged_scatter(term, axis_name):
    count = lax.axis_size(axis_name)
    if count % 4:
        return lax.psum_scatter(
            term.astype(jnp.bfloat16), axis_name, scatter_dimension=0, tiled=True
        ).astype(jnp.float32)
    block = term.shape[0] // count
    rest = term.shape[1:]
    sent = lax.optimization_barrier(term.astype(jnp.bfloat16))
    blocks = sent.reshape((count // 4, 2, 2, block) + rest)
    couples = [[low, low + 1] for low in range(0, count, 2)]
    first = swap_sum(jnp.moveaxis(blocks, 2, 0), axis_name, couples).astype(jnp.bfloat16)
    neighbours = [[low, low + 2] for low in range(count) if not (low >> 1) & 1]
    second = swap_sum(jnp.moveaxis(first, 1, 0), axis_name, neighbours).astype(jnp.bfloat16)
    others = [[high * 4 + low for high in range(count // 4)] for low in range(4)]
    return swap_sum(second, axis_name, others)


def body(cells, cotangent, row_weight, col_weight):
    row_saved = forward(cells, row_weight, 1, True)
    mid_columns = lax.all_to_all(row_saved[4], "cell", split_axis=1, concat_axis=0, tiled=True)
    col_saved = forward(mid_columns, col_weight, 0, False)
    grad_mid_columns, grad_col_proj = backward(col_saved, col_weight, cotangent, 0)
    col_pieces = weight_term(col_saved[1], grad_col_proj, col_saved[3], cotangent, 0)
    grad_mid = lax.all_to_all(grad_mid_columns, "cell", split_axis=0, concat_axis=1, tiled=True)
    grad_cells, grad_row_proj = backward(row_saved, row_weight, grad_mid, 1)
    row_pieces = weight_term(row_saved[1], grad_row_proj, row_saved[3], grad_mid, 1)
    early = jnp.concatenate(col_pieces + [row_pieces[1]], axis=1)
    early_grad = lax.psum_scatter(
        early.astype(jnp.bfloat16), "cell", scatter_dimension=0, tiled=True
    ).astype(jnp.float32)
    col_width = col_pieces[0].shape[1] + col_pieces[1].shape[1]
    col_grad = early_grad[:, :col_width]
    row_grad = jnp.concatenate([staged_scatter(row_pieces[0], "cell"), early_grad[:, col_width:]], axis=1)
    return (grad_cells, row_grad, col_grad)


def solution(mesh):
    placed = (P(("groups", "cell"), None, None), P("groups", "cell", None), P(), P())
    return jax.shard_map(
        body,
        mesh=mesh,
        in_specs=placed,
        out_specs=(
            P(("groups", "cell"), None, None),
            P(("groups", "cell"), None),
            P(("groups", "cell"), None),
        ),
        check_vma=False,
    )
```

```python
import jax
import jax.numpy as jnp
from jax import lax
from jax.sharding import PartitionSpec as P

HEADS = 12


EPS = 1e-06


def normalize(values):
    return values * lax.rsqrt(jnp.mean(values * values, axis=-1, keepdims=True) + EPS)


def attend_heads(queries, keys_part, values_part):
    head_size = queries.shape[-1]
    scores = jnp.einsum(
        "bhle,bhme->bhlm", queries, keys_part, preferred_element_type=jnp.float32
    ) * head_size ** (-0.5)
    weights = jax.nn.softmax(scores, axis=-1).astype(jnp.bfloat16)
    mixture = jnp.einsum("bhlm,bhme->bhle", weights, values_part, preferred_element_type=jnp.float32)
    return mixture.astype(jnp.bfloat16)


def forms_of(attn_dim):
    return "bld" if attn_dim == 1 else "lbd", "blf" if attn_dim == 1 else "lbf"


def split_weight(weight):
    model_width = weight.shape[0]
    head_size = model_width // HEADS
    projection = weight[:, : 3 * model_width].reshape(model_width, 3, HEADS, head_size)
    output = weight[:, 3 * model_width :].reshape(HEADS, head_size, model_width)
    return projection, output


def forward(cells_in, weight, attn_dim, with_result):
    cell_form, out_form = forms_of(attn_dim)
    projection, output = split_weight(weight)
    inputs_f = cells_in.astype(jnp.float32)
    normed = normalize(inputs_f).astype(jnp.bfloat16)
    projected = jnp.einsum(
        cell_form + ",dthe->tbhle", normed, projection, preferred_element_type=jnp.float32
    ).astype(jnp.bfloat16)
    attended = attend_heads(projected[0], projected[1], projected[2])
    result = None
    if with_result:
        result = (
            inputs_f
            + jnp.einsum("bhle,hef->" + out_form, attended, output, preferred_element_type=jnp.float32)
        ).astype(jnp.bfloat16)
    return (inputs_f, normed, projected, attended, result)


def backward(saved, weight, upstream, attn_dim):
    inputs_f, normed, projected, attended, result = saved
    cell_form, out_form = forms_of(attn_dim)
    projection, output = split_weight(weight)
    grad_attended = jnp.einsum(
        out_form + ",hef->bhle", upstream, output, preferred_element_type=jnp.float32
    ).astype(jnp.bfloat16)
    unused, pull = jax.vjp(attend_heads, projected[0], projected[1], projected[2])
    grad_projected = jnp.stack(pull(grad_attended)).astype(jnp.bfloat16)
    grad_normed = jnp.einsum(
        "tbhle,dthe->" + cell_form, grad_projected, projection, preferred_element_type=jnp.float32
    )
    unused_norm, pull_norm = jax.vjp(normalize, inputs_f)
    grad_input = (upstream.astype(jnp.float32) + pull_norm(grad_normed)[0]).astype(jnp.bfloat16)
    return (grad_input, grad_projected)


def weight_term(normed, grad_projected, attended, upstream, attn_dim):
    cell_form, out_form = forms_of(attn_dim)
    model_width = normed.shape[-1]
    first = jnp.einsum(
        cell_form + ",tbhle->dthe", normed, grad_projected, preferred_element_type=jnp.float32
    ).reshape(model_width, 3 * model_width)
    second = jnp.einsum(
        "bhle," + out_form + "->hef", attended, upstream, preferred_element_type=jnp.float32
    ).reshape(model_width, model_width)
    return jnp.concatenate([first, second], axis=1)


def swap_sum(parts, axis_name, groups):
    received = lax.all_to_all(parts, axis_name, split_axis=0, concat_axis=0, axis_index_groups=groups, tiled=True)
    total = received[0].astype(jnp.float32)
    for part in range(1, received.shape[0]):
        total = total + received[part].astype(jnp.float32)
    return total


def staged_scatter(term, axis_name):
    count = lax.axis_size(axis_name)
    bits = count.bit_length() - 1
    if count != 1 << bits or bits < 2:
        return lax.psum_scatter(
            term.astype(jnp.bfloat16), axis_name, scatter_dimension=0, tiled=True
        ).astype(jnp.float32)
    block = term.shape[0] // count
    sent = lax.optimization_barrier(term.astype(jnp.bfloat16))
    current = sent.reshape((2,) * bits + (block,) + term.shape[1:])
    remaining = list(range(bits - 1, -1, -1))
    order = [0] + list(range(2, bits)) + [1]
    for step, bit in enumerate(order):
        axis = remaining.index(bit)
        remaining.pop(axis)
        couples = [[low, low | (1 << bit)] for low in range(count) if not (low >> bit) & 1]
        total = swap_sum(jnp.moveaxis(current, axis, 0), axis_name, couples)
        current = total if step == bits - 1 else total.astype(jnp.bfloat16)
    return current


def body(cells, cotangent, row_weight, col_weight):
    row_saved = forward(cells, row_weight, 1, True)
    mid_columns = lax.all_to_all(row_saved[4], "cell", split_axis=1, concat_axis=0, tiled=True)
    col_saved = forward(mid_columns, col_weight, 0, False)
    grad_mid_columns, grad_col_proj = backward(col_saved, col_weight, cotangent, 0)
    col_term = weight_term(col_saved[1], grad_col_proj, col_saved[3], cotangent, 0)
    col_grad = lax.psum_scatter(
        col_term.astype(jnp.bfloat16), "cell", scatter_dimension=0, tiled=True
    ).astype(jnp.float32)
    grad_mid = lax.all_to_all(grad_mid_columns, "cell", split_axis=0, concat_axis=1, tiled=True)
    grad_cells, grad_row_proj = backward(row_saved, row_weight, grad_mid, 1)
    row_term = weight_term(row_saved[1], grad_row_proj, row_saved[3], grad_mid, 1)
    row_grad = staged_scatter(row_term, "cell")
    return (grad_cells, row_grad, col_grad)


def solution(mesh):
    placed = (P(("groups", "cell"), None, None), P("groups", "cell", None), P(), P())
    return jax.shard_map(
        body,
        mesh=mesh,
        in_specs=placed,
        out_specs=(
            P(("groups", "cell"), None, None),
            P(("groups", "cell"), None),
            P(("groups", "cell"), None),
        ),
        check_vma=False,
    )
```

```python
import jax
import jax.numpy as jnp
from jax import lax
from jax.sharding import PartitionSpec as P

HEADS = 12


EPS = 1e-06


def normalize(values):
    return values * lax.rsqrt(jnp.mean(values * values, axis=-1, keepdims=True) + EPS)


def attend_heads(queries, keys_part, values_part):
    head_size = queries.shape[-1]
    scores = jnp.einsum(
        "bhle,bhme->bhlm", queries, keys_part, preferred_element_type=jnp.float32
    ) * head_size ** (-0.5)
    weights = jax.nn.softmax(scores, axis=-1).astype(jnp.bfloat16)
    mixture = jnp.einsum("bhlm,bhme->bhle", weights, values_part, preferred_element_type=jnp.float32)
    return mixture.astype(jnp.bfloat16)


def forms_of(attn_dim):
    return "bld" if attn_dim == 1 else "lbd", "blf" if attn_dim == 1 else "lbf"


def split_weight(weight):
    model_width = weight.shape[0]
    head_size = model_width // HEADS
    projection = weight[:, : 3 * model_width].reshape(model_width, 3, HEADS, head_size)
    output = weight[:, 3 * model_width :].reshape(HEADS, head_size, model_width)
    return projection, output


def forward(cells_in, weight, attn_dim, with_result):
    cell_form, out_form = forms_of(attn_dim)
    projection, output = split_weight(weight)
    inputs_f = cells_in.astype(jnp.float32)
    normed = normalize(inputs_f).astype(jnp.bfloat16)
    projected = jnp.einsum(
        cell_form + ",dthe->tbhle", normed, projection, preferred_element_type=jnp.float32
    ).astype(jnp.bfloat16)
    attended = attend_heads(projected[0], projected[1], projected[2])
    result = None
    if with_result:
        result = (
            inputs_f
            + jnp.einsum("bhle,hef->" + out_form, attended, output, preferred_element_type=jnp.float32)
        ).astype(jnp.bfloat16)
    return (inputs_f, normed, projected, attended, result)


def backward(saved, weight, upstream, attn_dim):
    inputs_f, normed, projected, attended, result = saved
    cell_form, out_form = forms_of(attn_dim)
    projection, output = split_weight(weight)
    grad_attended = jnp.einsum(
        out_form + ",hef->bhle", upstream, output, preferred_element_type=jnp.float32
    ).astype(jnp.bfloat16)
    unused, pull = jax.vjp(attend_heads, projected[0], projected[1], projected[2])
    grad_projected = jnp.stack(pull(grad_attended)).astype(jnp.bfloat16)
    grad_normed = jnp.einsum(
        "tbhle,dthe->" + cell_form, grad_projected, projection, preferred_element_type=jnp.float32
    )
    unused_norm, pull_norm = jax.vjp(normalize, inputs_f)
    grad_input = (upstream.astype(jnp.float32) + pull_norm(grad_normed)[0]).astype(jnp.bfloat16)
    return (grad_input, grad_projected)


def weight_term(normed, grad_projected, attended, upstream, attn_dim):
    cell_form, out_form = forms_of(attn_dim)
    model_width = normed.shape[-1]
    first = jnp.einsum(
        cell_form + ",tbhle->dthe", normed, grad_projected, preferred_element_type=jnp.float32
    ).reshape(model_width, 3 * model_width)
    second = jnp.einsum(
        "bhle," + out_form + "->hef", attended, upstream, preferred_element_type=jnp.float32
    ).reshape(model_width, model_width)
    return [first, second]


def swap_sum(parts, axis_name, groups):
    received = lax.all_to_all(parts, axis_name, split_axis=0, concat_axis=0, axis_index_groups=groups, tiled=True)
    total = received[0].astype(jnp.float32)
    for part in range(1, received.shape[0]):
        total = total + received[part].astype(jnp.float32)
    return total


def staged_scatter(term, axis_name):
    count = lax.axis_size(axis_name)
    if count % 4:
        return lax.psum_scatter(
            term.astype(jnp.bfloat16), axis_name, scatter_dimension=0, tiled=True
        ).astype(jnp.float32)
    block = term.shape[0] // count
    rest = term.shape[1:]
    sent = lax.optimization_barrier(term.astype(jnp.bfloat16))
    blocks = sent.reshape((count // 4, 2, 2, block) + rest)
    couples = [[low, low + 1] for low in range(0, count, 2)]
    first = swap_sum(jnp.moveaxis(blocks, 2, 0), axis_name, couples).astype(jnp.bfloat16)
    neighbours = [[low, low + 2] for low in range(count) if not (low >> 1) & 1]
    second = swap_sum(jnp.moveaxis(first, 1, 0), axis_name, neighbours).astype(jnp.bfloat16)
    others = [[high * 4 + low for high in range(count // 4)] for low in range(4)]
    return swap_sum(second, axis_name, others)


def body(cells, cotangent, row_weight, col_weight):
    row_saved = forward(cells, row_weight, 1, True)
    mid_columns = lax.all_to_all(row_saved[4], "cell", split_axis=1, concat_axis=0, tiled=True)
    col_saved = forward(mid_columns, col_weight, 0, False)
    grad_mid_columns, grad_col_proj = backward(col_saved, col_weight, cotangent, 0)
    col_term = jnp.concatenate(weight_term(col_saved[1], grad_col_proj, col_saved[3], cotangent, 0), axis=1)
    col_grad = lax.psum_scatter(
        col_term.astype(jnp.bfloat16), "cell", scatter_dimension=0, tiled=True
    ).astype(jnp.float32)
    grad_mid = lax.all_to_all(grad_mid_columns, "cell", split_axis=0, concat_axis=1, tiled=True)
    grad_cells, grad_row_proj = backward(row_saved, row_weight, grad_mid, 1)
    row_pieces = weight_term(row_saved[1], grad_row_proj, row_saved[3], grad_mid, 1)
    early_grad = staged_scatter(row_pieces[1], "cell")
    early_grad, late_piece = lax.optimization_barrier((early_grad, row_pieces[0]))
    row_grad = jnp.concatenate([staged_scatter(late_piece, "cell"), early_grad], axis=1)
    return (grad_cells, row_grad, col_grad)


def solution(mesh):
    placed = (P(("groups", "cell"), None, None), P("groups", "cell", None), P(), P())
    return jax.shard_map(
        body,
        mesh=mesh,
        in_specs=placed,
        out_specs=(
            P(("groups", "cell"), None, None),
            P(("groups", "cell"), None),
            P(("groups", "cell"), None),
        ),
        check_vma=False,
    )
```
